768 devices in a mesh: row: 64 (over y, x, z_hi), col: 12 (over z_lo, core).
Axes of the slice: x: 4, y: 8, z: 12 (z_hi: 2, z_lo: 6; z = z_hi * 6 + z_lo), core: 2. Of those that a mesh axis runs over, the one named last changes fastest.
Arguments:
- node_features: bfloat16 [98304, 128], P(('row', 'col')), may hold values from -6 to 6
- weight: bfloat16 [128, 256], replicated, may hold values from -0.5 to 0.5
- block_values: bfloat16 [64, 12, 72, 128, 128], P('row', 'col'), may hold values from -0.21875 to 0.21875
- tile_rows: int32 [64, 12, 72], P('row', 'col'), may hold values from 0 to 11, as said below
- tile_cols: int32 [64, 12, 72], P('row', 'col'), may hold values from 0 to 63
- tile_count: int32 [64, 12], P('row', 'col'), may hold values from 18 to 72, as said below
- grad_out: bfloat16 [98304, 256], P(('row', 'col')), may hold values from -6 to 6
Outputs:
- activations: bfloat16 [98304, 256], P(('row', 'col'))
- grad_features: bfloat16 [98304, 128], P(('row', 'col'))
The draws below stay inside these ranges and needn't reach their ends.
Inputs may be any that keep to these rules, and one draw needn't show every extreme that they name: In each tile, the slots below tile_count name distinct pairs (tile_rows, tile_cols); later slots are not part of A. `tile_count`: some tile holds 72 used slots in every draw.
All inputs are finite; a program needn't handle non-finite values.
Results may differ from the reference program's by a relative error of at most 0.018.
Values may be sent and summed in bfloat16 or wider, within the bound.
No kernel may reach another device: no remote copies, remote signals or barrier semaphores. Data moves between devices by JAX's collectives and lax.ppermute only.
A program may use at most 64 MiB of HBM per device.

```python
import jax
import jax.numpy as jnp
from jax import lax

F_IN = 128
HID = 256
NODE_DEV = 128
BLK = 128
RBT = 12
CBT = 64
MAXB = 72
NODES = 98304
N_ROW = 64
N_COL = 12


def block_slots(key):
    base = jax.random.fold_in(key, 7)
    tile_keys = jax.random.split(base, N_ROW * N_COL)

    def one_tile(tile_key):
        return jax.random.permutation(tile_key, RBT * CBT)[:MAXB]
    chosen = jax.vmap(one_tile)(tile_keys)
    return chosen.reshape(N_ROW, N_COL, MAXB).astype(jnp.int32)


def draw_tile_rows(key, part):
    return (block_slots(key) // CBT).astype(jnp.int32)


def draw_tile_cols(key, part):
    return (block_slots(key) % CBT).astype(jnp.int32)


def draw_tile_count(key, part):
    counts = jax.random.randint(jax.random.fold_in(key, 11), (N_ROW * N_COL,), MAXB // 4, MAXB + 1)
    fullest = jax.random.randint(jax.random.fold_in(key, 13), (), 0, N_ROW * N_COL)
    counts = jnp.where(jnp.arange(N_ROW * N_COL) == fullest, MAXB, counts)
    return counts.reshape(N_ROW, N_COL).astype(jnp.int32)


def steps_of(key, extent, pieces, low, largest):
    factor_of = 1.0
    for dim, shards_of in pieces:
        heights = jax.random.uniform(jax.random.fold_in(jax.random.fold_in(key, 6), dim), (shards_of,), jnp.float32, low / len(pieces), largest / len(pieces))
        factor_of = factor_of * jnp.repeat(jnp.exp(heights), extent[dim] // shards_of).reshape((-1,) + (1,) * (len(extent) - 1 - dim))
    return factor_of


def centred(rng, shape, width, most, pieces=(), held_as=jnp.bfloat16):
    loudness = steps_of(rng, shape, pieces, -0.22, 0.18) if pieces else 1.0
    result = jax.random.normal(rng, shape, jnp.float32) * width * loudness
    return jnp.minimum(jnp.maximum(result, -most), most).astype(held_as)


def setup_inputs(seed: int = 0) -> dict:
    splits = jax.random.split(jax.random.key(seed), 8)
    node_features = centred(splits[0], (NODES, F_IN), 1.0, 6.0, ((0, 768),))
    weight = centred(splits[1], (F_IN, HID), F_IN ** -0.5, 0.5)
    block_values = centred(splits[2], (N_ROW, N_COL, MAXB, BLK, BLK), (max(1, MAXB // RBT) * BLK) ** -0.5, 0.21875, ((0, 64), (1, 12)))
    tile_rows = draw_tile_rows(jax.random.fold_in(splits[7], 71), 0)
    tile_cols = draw_tile_cols(jax.random.fold_in(splits[7], 71), 0)
    tile_count = draw_tile_count(jax.random.fold_in(splits[7], 71), 0)
    grad_out = centred(splits[6], (NODES, HID), 1.0, 6.0, ((0, 768),))
    return dict(node_features=node_features, weight=weight, block_values=block_values, tile_rows=tile_rows, tile_cols=tile_cols, tile_count=tile_count, grad_out=grad_out)


def tile_forward(values, row_ids, col_ids, tile_total, source, row_blocks):
    slots = values.shape[0]
    block_size = values.shape[1]
    feat_width = source.shape[-1]
    picked = jnp.take(source.reshape(-1, block_size, feat_width), col_ids, axis=0)
    product = jnp.einsum('bik,bkf->bif', values.astype(jnp.float32), picked.astype(jnp.float32))
    live_slot = jnp.arange(slots, dtype=jnp.int32) < tile_total
    select = ((row_ids[None, :] == jnp.arange(row_blocks, dtype=jnp.int32)[:, None]) & live_slot[None, :]).astype(jnp.float32)
    summed = jnp.einsum('rb,bif->rif', select, product, precision=lax.Precision.HIGHEST)
    return summed.reshape(row_blocks * block_size, feat_width)


def tile_backward(values, row_ids, col_ids, tile_total, source, col_blocks):
    slots = values.shape[0]
    block_size = values.shape[1]
    feat_width = source.shape[-1]
    picked = jnp.take(source.reshape(-1, block_size, feat_width), row_ids, axis=0)
    product = jnp.einsum('bki,bkf->bif', values.astype(jnp.float32), picked.astype(jnp.float32))
    live_slot = jnp.arange(slots, dtype=jnp.int32) < tile_total
    select = ((col_ids[None, :] == jnp.arange(col_blocks, dtype=jnp.int32)[:, None]) & live_slot[None, :]).astype(jnp.float32)
    summed = jnp.einsum('cb,bif->cif', select, product, precision=lax.Precision.HIGHEST)
    return summed.reshape(col_blocks * block_size, feat_width)


def silu_slope(pre):
    sigm = jax.nn.sigmoid(pre)
    return sigm * (1.0 + pre * (1.0 - sigm))


def reference(node_features, weight, block_values, tile_rows, tile_cols, tile_count, grad_out):
    transformed = jnp.dot(node_features, weight, preferred_element_type=jnp.float32).astype(jnp.bfloat16)
    grouped = transformed.reshape(N_ROW, N_COL, NODE_DEV, HID)
    columns = jnp.transpose(grouped, (1, 0, 2, 3)).reshape(N_COL, N_ROW * NODE_DEV, HID)

    def forward_row(index):
        def one_tile(values, row_ids, col_ids, tile_total, source):
            return tile_forward(values, row_ids, col_ids, tile_total, source, RBT)
        tiles = jax.vmap(one_tile)(block_values[index], tile_rows[index], tile_cols[index], tile_count[index], columns)
        return jnp.sum(tiles, axis=0)

    pre = lax.map(forward_row, jnp.arange(N_ROW, dtype=jnp.int32)).reshape(NODES, HID)
    activations = (pre * jax.nn.sigmoid(pre)).astype(jnp.bfloat16)
    pre_grad = (grad_out.astype(jnp.float32) * silu_slope(pre)).astype(jnp.bfloat16)
    back = jnp.dot(pre_grad, weight.T, preferred_element_type=jnp.float32).astype(jnp.bfloat16)
    rows_back = back.reshape(N_ROW, RBT * BLK, F_IN)

    def backward_col(index):
        def one_tile(values, row_ids, col_ids, tile_total, source):
            return tile_backward(values, row_ids, col_ids, tile_total, source, CBT)
        tiles = jax.vmap(one_tile)(block_values[:, index], tile_rows[:, index], tile_cols[:, index], tile_count[:, index], rows_back)
        return jnp.sum(tiles, axis=0)

    col_grad = lax.map(backward_col, jnp.arange(N_COL, dtype=jnp.int32))
    col_grad = col_grad.reshape(N_COL, N_ROW, NODE_DEV, F_IN)
    grad_features = jnp.transpose(col_grad, (1, 0, 2, 3)).reshape(NODES, F_IN).astype(jnp.bfloat16)
    return (activations, grad_features)
```

```python
import jax
import jax.numpy as jnp
from jax import lax
from jax.sharding import Mesh
from jax.sharding import PartitionSpec as P

PHYS = (("y", 8), ("x", 4), ("zh", 2), ("zl", 6), ("core", 2))
ALL = tuple(name for name, _ in PHYS)
ROW = ("y", "x", "zh")
COL = ("zl", "core")
XY = ("y", "x")


def tile_forward(values, row_ids, col_ids, tile_total, source, row_blocks):
    slots = values.shape[0]
    block_size = values.shape[1]
    feat_width = source.shape[-1]
    picked = jnp.take(source.reshape(-1, block_size, feat_width), col_ids, axis=0)
    product = jnp.einsum("bik,bkf->bif", values, picked, preferred_element_type=jnp.float32)
    live_slot = jnp.arange(slots, dtype=jnp.int32) < tile_total
    select = (
        (row_ids[None, :] == jnp.arange(row_blocks, dtype=jnp.int32)[:, None]) & live_slot[None, :]
    ).astype(jnp.float32)
    summed = jnp.einsum("rb,bif->rif", select, product, precision=lax.Precision.HIGHEST)
    return summed.reshape(row_blocks * block_size, feat_width)


def gather_columns(x):
    pair = lax.all_gather(x, "zh", axis=0, tiled=True)
    peers = lax.axis_size(XY)
    spread = jnp.broadcast_to(pair[None], (peers,) + pair.shape)
    return lax.all_to_all(spread, XY, 0, 0, tiled=False).reshape(-1, x.shape[1])


def scatter_rows(total, zh):
    peers = lax.axis_size(XY)
    parts = total.astype(jnp.bfloat16).reshape(peers, -1, total.shape[1])
    got = lax.all_to_all(parts, XY, 0, 0, tiled=False).astype(jnp.float32).sum(0)
    halves = got.reshape(2, -1, total.shape[1])
    mine = lax.dynamic_index_in_dim(halves, zh, 0, keepdims=False)
    other = lax.dynamic_index_in_dim(halves, 1 - zh, 0, keepdims=False)
    return mine + lax.ppermute(other, "zh", [(0, 1), (1, 0)])


def per_device(node_features, weight, block_values, tile_rows, tile_cols, tile_count, grad_out):
    block_size = block_values.shape[-1]
    values = block_values.reshape(-1, block_size, block_size)
    row_ids = tile_rows.reshape(-1)
    col_ids = tile_cols.reshape(-1)
    tile_total = tile_count.reshape(())
    node_rows = node_features.shape[0]
    feat_in = node_features.shape[1]
    n_col = lax.axis_size(COL)
    n_row = lax.axis_size(ROW)
    row_blocks = n_col * node_rows // block_size
    zh = lax.axis_index("zh")

    features = gather_columns(node_features)
    columns = jnp.dot(features, weight, preferred_element_type=jnp.float32).astype(jnp.bfloat16)
    partial_value = tile_forward(values, row_ids, col_ids, tile_total, columns, row_blocks)
    pieces = partial_value.astype(jnp.bfloat16).reshape(n_col, node_rows, -1)
    pre = lax.all_to_all(pieces, COL, 0, 0, tiled=False).astype(jnp.float32).sum(0)
    sigm = jax.nn.sigmoid(pre)
    activations = (pre * sigm).astype(jnp.bfloat16)
    pre_grad = (grad_out.astype(jnp.float32) * (sigm * (1.0 + pre * (1.0 - sigm)))).astype(
        jnp.bfloat16
    )
    back = jnp.dot(pre_grad, weight.T, preferred_element_type=jnp.float32).astype(jnp.bfloat16)
    rows_back = lax.all_gather(back, COL, axis=0, tiled=True)
    picked = jnp.take(rows_back.reshape(-1, block_size, feat_in), row_ids, axis=0)
    product = jnp.einsum("bki,bkf->bif", values, picked, preferred_element_type=jnp.float32)
    live_slot = jnp.arange(values.shape[0], dtype=jnp.int32) < tile_total
    select = (
        (
            col_ids[None, :]
            == jnp.arange(n_row * node_rows // block_size, dtype=jnp.int32)[:, None]
        )
        & live_slot[None, :]
    ).astype(jnp.float32)
    summed = jnp.einsum("cb,bif->cif", select, product, precision=lax.Precision.HIGHEST)
    grad_sum = scatter_rows(summed.reshape(n_row * node_rows, feat_in), zh)
    return (activations, grad_sum.astype(jnp.bfloat16))


def solution(mesh):
    sizes = tuple(size for _, size in PHYS)
    fine = Mesh(mesh.devices.reshape(sizes), ALL)
    placed = (
        P(ALL, None),
        P(),
        P(ROW, COL, None, None, None),
        P(ROW, COL, None),
        P(ROW, COL, None),
        P(ROW, COL),
        P(ALL, None),
    )
    return jax.shard_map(
        per_device,
        mesh=fine,
        in_specs=placed,
        out_specs=(P(ALL, None), P(ALL, None)),
        check_vma=False,
    )
```

```python
import jax
import jax.numpy as jnp
from jax import lax
from jax.sharding import Mesh
from jax.sharding import PartitionSpec as P
from jax.experimental import pallas as pl
from jax.experimental.pallas import tpu as pltpu

PHYS = (("y", 8), ("x", 4), ("zh", 2), ("zl", 6), ("core", 2))
ALL = tuple(name for name, _ in PHYS)
ROW = ("y", "x", "zh")
COL = ("zl", "core")
XY = ("y", "x")


def spmm_forward_kernel(rows_ref, cols_ref, count_ref, feat_ref, w_ref, vals_ref, out_ref, acc_ref):
    block = vals_ref.shape[1]
    acc_ref[...] = jnp.zeros_like(acc_ref)
    last_row = acc_ref.shape[0] // block - 1
    last_col = feat_ref.shape[0] // block - 1

    def body(s, carry):
        @pl.when(s < count_ref[0])
        def _():
            c = jnp.minimum(jnp.maximum(cols_ref[s], 0), last_col)
            r = jnp.minimum(jnp.maximum(rows_ref[s], 0), last_row)
            feat = feat_ref[pl.ds(pl.multiple_of(c * block, block), block), :]
            source = jnp.dot(feat, w_ref[...], preferred_element_type=jnp.float32).astype(
                jnp.bfloat16
            )
            rows = pl.ds(pl.multiple_of(r * block, block), block)
            acc_ref[rows, :] += jnp.dot(vals_ref[s], source, preferred_element_type=jnp.float32)

        return carry

    lax.fori_loop(0, vals_ref.shape[0], body, 0)
    out_ref[...] = acc_ref[...].astype(out_ref.dtype)


def spmm_backward_kernel(rows_ref, cols_ref, count_ref, back_ref, vals_ref, out_ref, acc_ref):
    block = vals_ref.shape[1]
    acc_ref[...] = jnp.zeros_like(acc_ref)
    last_row = back_ref.shape[0] // block - 1
    last_col = acc_ref.shape[0] // block - 1

    def body(s, carry):
        @pl.when(s < count_ref[0])
        def _():
            c = jnp.minimum(jnp.maximum(cols_ref[s], 0), last_col)
            r = jnp.minimum(jnp.maximum(rows_ref[s], 0), last_row)
            source = back_ref[pl.ds(pl.multiple_of(r * block, block), block), :]
            part = lax.dot_general(
                vals_ref[s], source, (((0,), (0,)), ((), ())), preferred_element_type=jnp.float32
            )
            cols = pl.ds(pl.multiple_of(c * block, block), block)
            acc_ref[cols, :] += part

        return carry

    lax.fori_loop(0, vals_ref.shape[0], body, 0)
    out_ref[...] = acc_ref[...].astype(out_ref.dtype)


def _specs(n_smem, n_vmem):
    return [pl.BlockSpec(memory_space=pltpu.SMEM)] * n_smem + [
        pl.BlockSpec(memory_space=pltpu.VMEM)
    ] * n_vmem


def spmm_forward(row_ids, col_ids, count, features, weight, values, row_blocks, interpret=False):
    block = values.shape[1]
    width = weight.shape[1]
    slots = values.shape[0]
    flops = slots * 2 * block * (features.shape[1] + block) * width
    return pl.pallas_call(
        spmm_forward_kernel,
        out_shape=jax.ShapeDtypeStruct((row_blocks * block, width), jnp.bfloat16),
        in_specs=_specs(3, 3),
        out_specs=pl.BlockSpec(memory_space=pltpu.VMEM),
        scratch_shapes=[pltpu.VMEM((row_blocks * block, width), jnp.float32)],
        cost_estimate=pl.CostEstimate(
            flops=flops,
            transcendentals=0,
            bytes_accessed=values.size * 2 + features.size * 2 + row_blocks * block * width * 2,
        ),
        interpret=interpret,
    )(row_ids, col_ids, count, features, weight, values)


def spmm_backward(row_ids, col_ids, count, back, values, col_blocks, interpret=False):
    block = values.shape[1]
    width = back.shape[1]
    slots = values.shape[0]
    return pl.pallas_call(
        spmm_backward_kernel,
        out_shape=jax.ShapeDtypeStruct((col_blocks * block, width), jnp.bfloat16),
        in_specs=_specs(3, 2),
        out_specs=pl.BlockSpec(memory_space=pltpu.VMEM),
        scratch_shapes=[pltpu.VMEM((col_blocks * block, width), jnp.float32)],
        cost_estimate=pl.CostEstimate(
            flops=slots * 2 * block * block * width,
            transcendentals=0,
            bytes_accessed=values.size * 2 + back.size * 2 + col_blocks * block * width * 2,
        ),
        interpret=interpret,
    )(row_ids, col_ids, count, back, values)


def gather_columns(x):
    pair = lax.all_gather(x, "zh", axis=0, tiled=True)
    peers = lax.axis_size(XY)
    spread = jnp.broadcast_to(pair[None], (peers,) + pair.shape)
    return lax.all_to_all(spread, XY, 0, 0, tiled=False).reshape(-1, x.shape[1])


def scatter_rows(total, zh):
    peers = lax.axis_size(XY)
    parts = total.astype(jnp.bfloat16).reshape(peers, -1, total.shape[1])
    got = lax.all_to_all(parts, XY, 0, 0, tiled=False).astype(jnp.float32).sum(0)
    halves = got.reshape(2, -1, total.shape[1])
    mine = lax.dynamic_index_in_dim(halves, zh, 0, keepdims=False)
    other = lax.dynamic_index_in_dim(halves, 1 - zh, 0, keepdims=False)
    return mine + lax.ppermute(other, "zh", [(0, 1), (1, 0)])


def per_device(node_features, weight, block_values, tile_rows, tile_cols, tile_count, grad_out):
    block_size = block_values.shape[-1]
    values = block_values.reshape(-1, block_size, block_size)
    row_ids = tile_rows.reshape(-1)
    col_ids = tile_cols.reshape(-1)
    node_rows = node_features.shape[0]
    n_col = lax.axis_size(COL)
    n_row = lax.axis_size(ROW)
    row_blocks = n_col * node_rows // block_size
    zh = lax.axis_index("zh")

    count = tile_count.reshape(1)
    features = gather_columns(node_features)
    partial_value = spmm_forward(row_ids, col_ids, count, features, weight, values, row_blocks)
    pieces = partial_value.reshape(n_col, node_rows, -1)
    pre = lax.all_to_all(pieces, COL, 0, 0, tiled=False).astype(jnp.float32).sum(0)
    sigm = jax.nn.sigmoid(pre)
    activations = (pre * sigm).astype(jnp.bfloat16)
    pre_grad = (grad_out.astype(jnp.float32) * (sigm * (1.0 + pre * (1.0 - sigm)))).astype(
        jnp.bfloat16
    )
    back = jnp.dot(pre_grad, weight.T, preferred_element_type=jnp.float32).astype(jnp.bfloat16)
    rows_back = lax.all_gather(back, COL, axis=0, tiled=True)
    summed = spmm_backward(row_ids, col_ids, count, rows_back, values, n_row * node_rows // block_size)
    grad_sum = scatter_rows(summed, zh)
    return (activations, grad_sum.astype(jnp.bfloat16))


def solution(mesh):
    sizes = tuple(size for _, size in PHYS)
    fine = Mesh(mesh.devices.reshape(sizes), ALL)
    placed = (
        P(ALL, None),
        P(),
        P(ROW, COL, None, None, None),
        P(ROW, COL, None),
        P(ROW, COL, None),
        P(ROW, COL),
        P(ALL, None),
    )
    return jax.shard_map(
        per_device,
        mesh=fine,
        in_specs=placed,
        out_specs=(P(ALL, None), P(ALL, None)),
        check_vma=False,
    )
```

```python
import jax
import jax.numpy as jnp
from jax import lax
from jax.sharding import Mesh
from jax.sharding import PartitionSpec as P
from jax.experimental import pallas as pl
from jax.experimental.pallas import tpu as pltpu

PHYS = (("y", 8), ("x", 4), ("zh", 2), ("zl", 6), ("core", 2))
ALL = tuple(name for name, _ in PHYS)
ROW = ("y", "x", "zh")
COL = ("zl", "core")
XY = ("y", "x")


def spmm_forward_kernel(rows_ref, cols_ref, count_ref, feat_ref, vals_ref, out_ref, acc_ref):
    block = vals_ref.shape[1]
    acc_ref[...] = jnp.zeros_like(acc_ref)
    last_row = acc_ref.shape[0] // block - 1
    last_col = feat_ref.shape[0] // block - 1

    def body(s, carry):
        c = jnp.minimum(jnp.maximum(cols_ref[s], 0), last_col)
        r = jnp.minimum(jnp.maximum(rows_ref[s], 0), last_row)
        feat = feat_ref[pl.ds(pl.multiple_of(c * block, block), block), :]
        part = jnp.dot(vals_ref[s], feat, preferred_element_type=jnp.float32)
        rows = pl.ds(pl.multiple_of(r * block, block), block)
        acc_ref[rows, :] += jnp.where(s < count_ref[0], part, 0.0)
        return carry

    lax.fori_loop(0, vals_ref.shape[0], body, 0, unroll=8)
    out_ref[...] = acc_ref[...].astype(out_ref.dtype)


def spmm_backward_kernel(rows_ref, cols_ref, count_ref, back_ref, vals_ref, out_ref, acc_ref):
    block = vals_ref.shape[1]
    acc_ref[...] = jnp.zeros_like(acc_ref)
    last_row = back_ref.shape[0] // block - 1
    last_col = acc_ref.shape[0] // block - 1

    def body(s, carry):
        c = jnp.minimum(jnp.maximum(cols_ref[s], 0), last_col)
        r = jnp.minimum(jnp.maximum(rows_ref[s], 0), last_row)
        source = back_ref[pl.ds(pl.multiple_of(r * block, block), block), :]
        part = lax.dot_general(
            vals_ref[s], source, (((0,), (0,)), ((), ())), preferred_element_type=jnp.float32
        )
        cols = pl.ds(pl.multiple_of(c * block, block), block)
        acc_ref[cols, :] += jnp.where(s < count_ref[0], part, 0.0)
        return carry

    lax.fori_loop(0, vals_ref.shape[0], body, 0, unroll=8)
    out_ref[...] = acc_ref[...].astype(out_ref.dtype)


def _specs(n_smem, n_vmem):
    return [pl.BlockSpec(memory_space=pltpu.SMEM)] * n_smem + [
        pl.BlockSpec(memory_space=pltpu.VMEM)
    ] * n_vmem


def spmm_forward(row_ids, col_ids, count, features, values, row_blocks, interpret=False):
    block = values.shape[1]
    width = features.shape[1]
    slots = values.shape[0]
    return pl.pallas_call(
        spmm_forward_kernel,
        out_shape=jax.ShapeDtypeStruct((row_blocks * block, width), jnp.bfloat16),
        in_specs=_specs(3, 2),
        out_specs=pl.BlockSpec(memory_space=pltpu.VMEM),
        scratch_shapes=[pltpu.VMEM((row_blocks * block, width), jnp.float32)],
        cost_estimate=pl.CostEstimate(
            flops=slots * 2 * block * block * width,
            transcendentals=0,
            bytes_accessed=values.size * 2 + features.size * 2 + row_blocks * block * width * 2,
        ),
        interpret=interpret,
    )(row_ids, col_ids, count, features, values)


def spmm_backward(row_ids, col_ids, count, back, values, col_blocks, interpret=False):
    block = values.shape[1]
    width = back.shape[1]
    slots = values.shape[0]
    return pl.pallas_call(
        spmm_backward_kernel,
        out_shape=jax.ShapeDtypeStruct((col_blocks * block, width), jnp.bfloat16),
        in_specs=_specs(3, 2),
        out_specs=pl.BlockSpec(memory_space=pltpu.VMEM),
        scratch_shapes=[pltpu.VMEM((col_blocks * block, width), jnp.float32)],
        cost_estimate=pl.CostEstimate(
            flops=slots * 2 * block * block * width,
            transcendentals=0,
            bytes_accessed=values.size * 2 + back.size * 2 + col_blocks * block * width * 2,
        ),
        interpret=interpret,
    )(row_ids, col_ids, count, back, values)


def gather_columns(x):
    pair = lax.all_gather(x, "zh", axis=0, tiled=True)
    peers = lax.axis_size(XY)
    spread = jnp.broadcast_to(pair[None], (peers,) + pair.shape)
    return lax.all_to_all(spread, XY, 0, 0, tiled=False).reshape(-1, x.shape[1])


def scatter_rows(total, zh):
    peers = lax.axis_size(XY)
    parts = total.astype(jnp.bfloat16).reshape(peers, -1, total.shape[1])
    got = lax.all_to_all(parts, XY, 0, 0, tiled=False).astype(jnp.float32).sum(0)
    halves = got.reshape(2, -1, total.shape[1])
    mine = lax.dynamic_index_in_dim(halves, zh, 0, keepdims=False)
    other = lax.dynamic_index_in_dim(halves, 1 - zh, 0, keepdims=False)
    return mine + lax.ppermute(other, "zh", [(0, 1), (1, 0)])


def per_device(node_features, weight, block_values, tile_rows, tile_cols, tile_count, grad_out):
    block_size = block_values.shape[-1]
    values = block_values.reshape(-1, block_size, block_size)
    row_ids = tile_rows.reshape(-1)
    col_ids = tile_cols.reshape(-1)
    node_rows = node_features.shape[0]
    n_col = lax.axis_size(COL)
    n_row = lax.axis_size(ROW)
    row_blocks = n_col * node_rows // block_size
    zh = lax.axis_index("zh")

    count = tile_count.reshape(1)
    features = gather_columns(node_features)
    partial_value = spmm_forward(row_ids, col_ids, count, features, values, row_blocks)
    pieces = partial_value.reshape(n_col, node_rows, -1)
    aggregated = lax.all_to_all(pieces, COL, 0, 0, tiled=False).astype(jnp.float32).sum(0)
    pre = jnp.dot(aggregated, weight.astype(jnp.float32), precision=lax.Precision.HIGHEST)
    sigm = jax.nn.sigmoid(pre)
    activations = (pre * sigm).astype(jnp.bfloat16)
    pre_grad = (grad_out.astype(jnp.float32) * (sigm * (1.0 + pre * (1.0 - sigm)))).astype(
        jnp.bfloat16
    )
    back = jnp.dot(pre_grad, weight.T, preferred_element_type=jnp.float32).astype(jnp.bfloat16)
    rows_back = lax.all_gather(back, COL, axis=0, tiled=True)
    summed = spmm_backward(row_ids, col_ids, count, rows_back, values, n_row * node_rows // block_size)
    grad_sum = scatter_rows(summed, zh)
    return (activations, grad_sum.astype(jnp.bfloat16))


def solution(mesh):
    sizes = tuple(size for _, size in PHYS)
    fine = Mesh(mesh.devices.reshape(sizes), ALL)
    placed = (
        P(ALL, None),
        P(),
        P(ROW, COL, None, None, None),
        P(ROW, COL, None),
        P(ROW, COL, None),
        P(ROW, COL),
        P(ALL, None),
    )
    return jax.shard_map(
        per_device,
        mesh=fine,
        in_specs=placed,
        out_specs=(P(ALL, None), P(ALL, None)),
        check_vma=False,
    )
```

```python
import jax
import jax.numpy as jnp
from jax import lax
from jax.sharding import Mesh
from jax.sharding import PartitionSpec as P
from jax.experimental import pallas as pl
from jax.experimental.pallas import tpu as pltpu

PHYS = (("y", 8), ("x", 4), ("zh", 2), ("zl", 6), ("core", 2))
ALL = tuple(name for name, _ in PHYS)
ROW = ("y", "x", "zh")
COL = ("zl", "core")
XY = ("y", "x")


def spmm_forward_kernel(rows_ref, cols_ref, count_ref, feat_ref, vals_ref, out_ref, acc_ref):
    block = vals_ref.shape[1]
    acc_ref[...] = jnp.zeros_like(acc_ref)
    last_row = acc_ref.shape[0] // block - 1
    last_col = feat_ref.shape[0] // block - 1

    def body(s, carry):
        c = jnp.minimum(jnp.maximum(cols_ref[s], 0), last_col)
        r = jnp.minimum(jnp.maximum(rows_ref[s], 0), last_row)
        feat = feat_ref[pl.ds(pl.multiple_of(c * block, block), block), :]
        part = jnp.dot(vals_ref[s], feat, preferred_element_type=jnp.float32)
        rows = pl.ds(pl.multiple_of(r * block, block), block)
        acc_ref[rows, :] += jnp.where(s < count_ref[0], part, 0.0)
        return carry

    lax.fori_loop(0, vals_ref.shape[0], body, 0, unroll=True)
    out_ref[...] = acc_ref[...].astype(out_ref.dtype)


def spmm_backward_kernel(rows_ref, cols_ref, count_ref, back_ref, vals_ref, out_ref, acc_ref):
    block = vals_ref.shape[1]
    acc_ref[...] = jnp.zeros_like(acc_ref)
    last_row = back_ref.shape[0] // block - 1
    last_col = acc_ref.shape[0] // block - 1

    def body(s, carry):
        c = jnp.minimum(jnp.maximum(cols_ref[s], 0), last_col)
        r = jnp.minimum(jnp.maximum(rows_ref[s], 0), last_row)
        source = back_ref[pl.ds(pl.multiple_of(r * block, block), block), :]
        part = lax.dot_general(
            vals_ref[s], source, (((0,), (0,)), ((), ())), preferred_element_type=jnp.float32
        )
        cols = pl.ds(pl.multiple_of(c * block, block), block)
        acc_ref[cols, :] += jnp.where(s < count_ref[0], part, 0.0)
        return carry

    lax.fori_loop(0, vals_ref.shape[0], body, 0, unroll=True)
    out_ref[...] = acc_ref[...].astype(out_ref.dtype)


def _specs(n_smem, n_vmem):
    return [pl.BlockSpec(memory_space=pltpu.SMEM)] * n_smem + [
        pl.BlockSpec(memory_space=pltpu.VMEM)
    ] * n_vmem


def spmm_forward(row_ids, col_ids, count, features, values, row_blocks, interpret=False):
    block = values.shape[1]
    width = features.shape[1]
    slots = values.shape[0]
    return pl.pallas_call(
        spmm_forward_kernel,
        out_shape=jax.ShapeDtypeStruct((row_blocks * block, width), jnp.bfloat16),
        in_specs=_specs(3, 2),
        out_specs=pl.BlockSpec(memory_space=pltpu.VMEM),
        scratch_shapes=[pltpu.VMEM((row_blocks * block, width), jnp.float32)],
        cost_estimate=pl.CostEstimate(
            flops=slots * 2 * block * block * width,
            transcendentals=0,
            bytes_accessed=values.size * 2 + features.size * 2 + row_blocks * block * width * 2,
        ),
        interpret=interpret,
    )(row_ids, col_ids, count, features, values)


def spmm_backward(row_ids, col_ids, count, back, values, col_blocks, interpret=False):
    block = values.shape[1]
    width = back.shape[1]
    slots = values.shape[0]
    return pl.pallas_call(
        spmm_backward_kernel,
        out_shape=jax.ShapeDtypeStruct((col_blocks * block, width), jnp.bfloat16),
        in_specs=_specs(3, 2),
        out_specs=pl.BlockSpec(memory_space=pltpu.VMEM),
        scratch_shapes=[pltpu.VMEM((col_blocks * block, width), jnp.float32)],
        cost_estimate=pl.CostEstimate(
            flops=slots * 2 * block * block * width,
            transcendentals=0,
            bytes_accessed=values.size * 2 + back.size * 2 + col_blocks * block * width * 2,
        ),
        interpret=interpret,
    )(row_ids, col_ids, count, back, values)


def gather_columns(x):
    pair = lax.all_gather(x, "zh", axis=0, tiled=True)
    peers = lax.axis_size(XY)
    spread = jnp.broadcast_to(pair[None], (peers,) + pair.shape)
    return lax.all_to_all(spread, XY, 0, 0, tiled=False).reshape(-1, x.shape[1])


def scatter_rows(total, zh):
    peers = lax.axis_size(XY)
    parts = total.astype(jnp.bfloat16).reshape(peers, -1, total.shape[1])
    got = lax.all_to_all(parts, XY, 0, 0, tiled=False).astype(jnp.float32).sum(0)
    halves = got.reshape(2, -1, total.shape[1])
    mine = lax.dynamic_index_in_dim(halves, zh, 0, keepdims=False)
    other = lax.dynamic_index_in_dim(halves, 1 - zh, 0, keepdims=False)
    return mine + lax.ppermute(other, "zh", [(0, 1), (1, 0)])


def per_device(node_features, weight, block_values, tile_rows, tile_cols, tile_count, grad_out):
    block_size = block_values.shape[-1]
    values = block_values.reshape(-1, block_size, block_size)
    row_ids = tile_rows.reshape(-1)
    col_ids = tile_cols.reshape(-1)
    node_rows = node_features.shape[0]
    n_col = lax.axis_size(COL)
    n_row = lax.axis_size(ROW)
    row_blocks = n_col * node_rows // block_size
    zh = lax.axis_index("zh")

    count = tile_count.reshape(1)
    features = gather_columns(node_features)
    partial_value = spmm_forward(row_ids, col_ids, count, features, values, row_blocks)
    pieces = partial_value.reshape(n_col, node_rows, -1)
    aggregated = lax.all_to_all(pieces, COL, 0, 0, tiled=False).astype(jnp.float32).sum(0)
    pre = jnp.dot(aggregated, weight.astype(jnp.float32), precision=lax.Precision.HIGHEST)
    sigm = jax.nn.sigmoid(pre)
    activations = (pre * sigm).astype(jnp.bfloat16)
    pre_grad = (grad_out.astype(jnp.float32) * (sigm * (1.0 + pre * (1.0 - sigm)))).astype(
        jnp.bfloat16
    )
    back = jnp.dot(pre_grad, weight.T, preferred_element_type=jnp.float32).astype(jnp.bfloat16)
    rows_back = lax.all_gather(back, COL, axis=0, tiled=True)
    summed = spmm_backward(row_ids, col_ids, count, rows_back, values, n_row * node_rows // block_size)
    grad_sum = scatter_rows(summed, zh)
    return (activations, grad_sum.astype(jnp.bfloat16))


def solution(mesh):
    sizes = tuple(size for _, size in PHYS)
    fine = Mesh(mesh.devices.reshape(sizes), ALL)
    placed = (
        P(ALL, None),
        P(),
        P(ROW, COL, None, None, None),
        P(ROW, COL, None),
        P(ROW, COL, None),
        P(ROW, COL),
        P(ALL, None),
    )
    return jax.shard_map(
        per_device,
        mesh=fine,
        in_specs=placed,
        out_specs=(P(ALL, None), P(ALL, None)),
        check_vma=False,
    )
```

```python
import jax
import jax.numpy as jnp
from jax import lax
from jax.sharding import Mesh
from jax.sharding import PartitionSpec as P
from jax.experimental import pallas as pl
from jax.experimental.pallas import tpu as pltpu

PHYS = (("y", 8), ("x", 4), ("zh", 2), ("zl", 6), ("core", 2))
ALL = tuple(name for name, _ in PHYS)
ROW = ("y", "x", "zh")
COL = ("zl", "core")
XY = ("y", "x")


def spmm_forward_kernel(rows_ref, cols_ref, count_ref, feat_ref, vals_ref, out_ref, acc_ref):
    block = vals_ref.shape[1]
    acc_ref[...] = jnp.zeros_like(acc_ref)
    last_row = acc_ref.shape[0] // block - 1
    last_col = feat_ref.shape[0] // block - 1

    def body(s, carry):
        c = jnp.minimum(jnp.maximum(cols_ref[s], 0), last_col)
        r = jnp.minimum(jnp.maximum(rows_ref[s], 0), last_row)
        feat = feat_ref[pl.ds(pl.multiple_of(c * block, block), block), :]
        part = jnp.dot(vals_ref[s], feat, preferred_element_type=jnp.float32)
        rows = pl.ds(pl.multiple_of(r * block, block), block)
        acc_ref[rows, :] += jnp.where(s < count_ref[0], part, 0.0)
        return carry

    lax.fori_loop(0, vals_ref.shape[0], body, 0, unroll=True)
    out_ref[...] = acc_ref[...].astype(out_ref.dtype)


def spmm_backward_kernel(rows_ref, cols_ref, count_ref, back_ref, vals_ref, out_ref, acc_ref):
    block = vals_ref.shape[1]
    acc_ref[...] = jnp.zeros_like(acc_ref)
    last_row = back_ref.shape[0] // block - 1
    last_col = acc_ref.shape[0] // block - 1

    def body(s, carry):
        c = jnp.minimum(jnp.maximum(cols_ref[s], 0), last_col)
        r = jnp.minimum(jnp.maximum(rows_ref[s], 0), last_row)
        source = back_ref[pl.ds(pl.multiple_of(r * block, block), block), :]
        part = lax.dot_general(
            vals_ref[s], source, (((0,), (0,)), ((), ())), preferred_element_type=jnp.float32
        )
        cols = pl.ds(pl.multiple_of(c * block, block), block)
        acc_ref[cols, :] += jnp.where(s < count_ref[0], part, 0.0)
        return carry

    lax.fori_loop(0, vals_ref.shape[0], body, 0, unroll=True)
    out_ref[...] = acc_ref[...].astype(out_ref.dtype)


def _specs(n_smem, n_vmem):
    return [pl.BlockSpec(memory_space=pltpu.SMEM)] * n_smem + [
        pl.BlockSpec(memory_space=pltpu.VMEM)
    ] * n_vmem


def spmm_forward(row_ids, col_ids, count, features, values, row_blocks, interpret=False):
    block = values.shape[1]
    width = features.shape[1]
    slots = values.shape[0]
    return pl.pallas_call(
        spmm_forward_kernel,
        out_shape=jax.ShapeDtypeStruct((row_blocks * block, width), jnp.bfloat16),
        in_specs=_specs(3, 2),
        out_specs=pl.BlockSpec(memory_space=pltpu.VMEM),
        scratch_shapes=[pltpu.VMEM((row_blocks * block, width), jnp.float32)],
        cost_estimate=pl.CostEstimate(
            flops=slots * 2 * block * block * width,
            transcendentals=0,
            bytes_accessed=values.size * 2 + features.size * 2 + row_blocks * block * width * 2,
        ),
        interpret=interpret,
    )(row_ids, col_ids, count, features, values)


def spmm_backward(row_ids, col_ids, count, back, values, col_blocks, interpret=False):
    block = values.shape[1]
    width = back.shape[1]
    slots = values.shape[0]
    return pl.pallas_call(
        spmm_backward_kernel,
        out_shape=jax.ShapeDtypeStruct((col_blocks * block, width), jnp.bfloat16),
        in_specs=_specs(3, 2),
        out_specs=pl.BlockSpec(memory_space=pltpu.VMEM),
        scratch_shapes=[pltpu.VMEM((col_blocks * block, width), jnp.float32)],
        cost_estimate=pl.CostEstimate(
            flops=slots * 2 * block * block * width,
            transcendentals=0,
            bytes_accessed=values.size * 2 + back.size * 2 + col_blocks * block * width * 2,
        ),
        interpret=interpret,
    )(row_ids, col_ids, count, back, values)


def gather_columns(x):
    pair = lax.all_gather(x, "zh", axis=0, tiled=True)
    peers = lax.axis_size(XY)
    spread = jnp.broadcast_to(pair[None], (peers,) + pair.shape)
    return lax.all_to_all(spread, XY, 0, 0, tiled=False).reshape(-1, x.shape[1])


def scatter_rows(total, zh):
    peers = lax.axis_size(XY)
    parts = total.astype(jnp.bfloat16).reshape(peers, -1, total.shape[1])
    got = lax.all_to_all(parts, XY, 0, 0, tiled=False).astype(jnp.float32).sum(0)
    halves = got.reshape(2, -1, total.shape[1])
    mine = lax.dynamic_index_in_dim(halves, zh, 0, keepdims=False)
    other = lax.dynamic_index_in_dim(halves, 1 - zh, 0, keepdims=False)
    swapped = lax.all_gather(other, "zh", axis=0, tiled=False)
    return mine + lax.dynamic_index_in_dim(swapped, 1 - zh, 0, keepdims=False)


def per_device(node_features, weight, block_values, tile_rows, tile_cols, tile_count, grad_out):
    block_size = block_values.shape[-1]
    values = block_values.reshape(-1, block_size, block_size)
    row_ids = tile_rows.reshape(-1)
    col_ids = tile_cols.reshape(-1)
    node_rows = node_features.shape[0]
    n_col = lax.axis_size(COL)
    n_row = lax.axis_size(ROW)
    row_blocks = n_col * node_rows // block_size
    zh = lax.axis_index("zh")

    count = tile_count.reshape(1)
    features = gather_columns(node_features)
    partial_value = spmm_forward(row_ids, col_ids, count, features, values, row_blocks)
    pieces = partial_value.reshape(n_col, node_rows, -1)
    aggregated = lax.all_to_all(pieces, COL, 0, 0, tiled=False).astype(jnp.float32).sum(0)
    pre = jnp.dot(aggregated, weight.astype(jnp.float32), precision=lax.Precision.HIGHEST)
    sigm = jax.nn.sigmoid(pre)
    activations = (pre * sigm).astype(jnp.bfloat16)
    pre_grad = (grad_out.astype(jnp.float32) * (sigm * (1.0 + pre * (1.0 - sigm)))).astype(
        jnp.bfloat16
    )
    back = jnp.dot(pre_grad, weight.T, preferred_element_type=jnp.float32).astype(jnp.bfloat16)
    rows_back = lax.all_gather(back, COL, axis=0, tiled=True)
    summed = spmm_backward(row_ids, col_ids, count, rows_back, values, n_row * node_rows // block_size)
    grad_sum = scatter_rows(summed, zh)
    return (activations, grad_sum.astype(jnp.bfloat16))


def solution(mesh):
    sizes = tuple(size for _, size in PHYS)
    fine = Mesh(mesh.devices.reshape(sizes), ALL)
    placed = (
        P(ALL, None),
        P(),
        P(ROW, COL, None, None, None),
        P(ROW, COL, None),
        P(ROW, COL, None),
        P(ROW, COL),
        P(ALL, None),
    )
    return jax.shard_map(
        per_device,
        mesh=fine,
        in_specs=placed,
        out_specs=(P(ALL, None), P(ALL, None)),
        check_vma=False,
    )
```
